32 devices in a mesh: groups: 2 (over y), space: 16 (over z, x, core).
Axes of the slice: x: 2, y: 2, z: 4, core: 2. Of those that a mesh axis runs over, the one named last changes fastest.
Arguments:
- field: float32 [64, 40, 8, 256], P(('groups', 'space')), parts along dimension 0, may hold values from -6 to 6
- grad_out: float32 [64, 40, 8, 256], P(('groups', 'space')), parts along dimension 0, may hold values from -6 to 6
- weight: float32 [256, 27, 256], P('space'), may hold values from -0.078125 to 0.078125
- bias: float32 [256], replicated, may hold values from -3 to 3
- land_bias: float32 [256], replicated, may hold values from -3 to 3
- level_gain: float32 [4, 256], replicated, may hold values from 0.5 to 1.5
- land_mask: int32 [32, 40], P('space'), may hold values 0 or 1
- level_index: int32 [8], replicated, may hold values from 0 to 3, as said below
Outputs:
- grad_field: float32 [64, 40, 8, 256], P(('groups', 'space')), parts along dimension 0
- grad_weight: float32 [512, 27, 256], P(('groups', 'space')), parts along dimension 0
- grad_bias: float32 [512], P('groups'), parts along dimension 0
- grad_land: float32 [512], P('groups'), parts along dimension 0
- grad_gain: float32 [8, 256], P('groups'), parts along dimension 0
The draws below stay inside these ranges and needn't reach their ends.
There are 2 independent parts, one for each index of `groups`. The reference program is written for one: setup_inputs(seed, part) draws one part's arguments, and reference() takes and returns one part's arrays. A program takes and returns all parts, laid end to end along the dimension named above; an argument that names none is the same for every part. Nothing has to cross between parts.
Inputs may be any that keep to these rules, and one draw needn't show every extreme that they name: `level_index`: a gain table row for each level; every row of the table is used by some level.
All inputs are finite; a program needn't handle non-finite values. No bound on the sum of `land_mask` on one device may be relied on, other than what follows from the above.
Results may differ from the reference program's by a relative error of at most 0.00011.
Values sent between devices are 32-bit elements; how exact they have to be, the bound alone decides.
No kernel may reach another device: no remote copies, remote signals or barrier semaphores. Data moves between devices by JAX's collectives and lax.ppermute only.
A program may use at most 128 MiB of HBM per device.

```python
import jax
import jax.numpy as jnp
from jax import lax

C = 256
LON = 40
LEV = 8
NCOEF = 4
LAT = 32


def draw_level_index(key, part):
    first_key = jax.random.fold_in(key, 11)
    second_key = jax.random.fold_in(key, 12)
    third_key = jax.random.fold_in(key, 13)
    base_rows = jax.random.randint(first_key, (LEV,), 0, NCOEF).astype(jnp.int32)
    chosen = jax.random.permutation(second_key, LEV)[:NCOEF]
    ordered = jax.random.permutation(third_key, NCOEF).astype(jnp.int32)
    return base_rows.at[chosen].set(ordered).astype(jnp.int32)


def touch_ends(entries, own_key, smallest, high):
    longest = entries.shape.index(max(entries.shape))
    spots = []
    for shift in (0, 1):
        where = [jax.random.randint(jax.random.fold_in(own_key, axis), (), 0, length) for axis, length in enumerate(entries.shape)]
        where[longest] = (where[longest] + shift) % entries.shape[longest]
        spots.append(tuple(where))
    return entries.at[spots[0]].set(smallest).at[spots[1]].set(high)


def steps_of(stream_key, shape, cuts, low, largest):
    factor_of = 1.0
    for dim, parts in cuts:
        draws = jax.random.uniform(jax.random.fold_in(jax.random.fold_in(stream_key, 6), dim), (parts,), jnp.float32, low / len(cuts), largest / len(cuts))
        factor_of = factor_of * jnp.repeat(jnp.exp(draws), shape[dim] // parts).reshape((-1,) + (1,) * (len(shape) - 1 - dim))
    return factor_of


def scatter_about(key, dims, spread, most, split=(), held_as=jnp.bfloat16):
    factor_of = steps_of(key, dims, split, -0.22, 0.18) if split else 1.0
    drawn = jax.random.normal(key, dims, jnp.float32) * spread * factor_of
    return jnp.minimum(jnp.maximum(drawn, -most), most).astype(held_as)


def setup_inputs(seed: int = 0, part: int = 0) -> dict:
    splits = jax.random.split(jax.random.key(seed), 9)
    part_keys = jax.random.split(jax.random.fold_in(splits[8], part), 9)
    return {
        "field": scatter_about(part_keys[0], (LAT, LON, LEV, C), 1.0, 6.0, ((0, 16),), jnp.float32),
        "grad_out": scatter_about(part_keys[1], (LAT, LON, LEV, C), 1.0, 6.0, ((0, 16),), jnp.float32),
        "weight": scatter_about(splits[2], (C, 27, C), (27 * C) ** -0.5, 0.078125, ((0, 16),), jnp.float32),
        "bias": scatter_about(splits[3], (C,), 0.5, 3.0, (), jnp.float32),
        "land_bias": scatter_about(splits[4], (C,), 0.5, 3.0, (), jnp.float32),
        "level_gain": jnp.clip(jax.random.uniform(splits[5], (NCOEF, C), jnp.float32, 0.5, 1.5), 0.5, 1.5),
        "land_mask": touch_ends((jax.random.randint(splits[6], (LAT, LON), 0, 10) < 3).astype(jnp.int32), jax.random.fold_in(splits[6], 1), 0, 1),
        "level_index": draw_level_index(jax.random.fold_in(splits[8], 71), part),
    }


def extend_grid(field):
    wrapped = jnp.concatenate([field[:, -1:], field, field[:, :1]], axis=1)
    return jnp.pad(wrapped, ((1, 1), (0, 0), (1, 1), (0, 0)))

def forward(field, weight, bias, land_bias, level_gain, land_float, one_hot):
    padded = extend_grid(field)
    chans = field.shape[3]
    kernel = jnp.transpose(weight.reshape(chans, 3, 3, 3, chans), (1, 2, 3, 0, 4))
    conv = lax.conv_general_dilated(padded[None], kernel, (1, 1, 1), 'VALID', dimension_numbers=('NDHWC', 'DHWIO', 'NDHWC'), precision=lax.Precision.HIGHEST)[0]
    pre = conv + bias + land_float[:, :, None, None] * land_bias
    gains = jnp.dot(one_hot, level_gain, precision=lax.Precision.HIGHEST)
    return field + gains * jax.nn.silu(pre)

def reference(field, grad_out, weight, bias, land_bias, level_gain, land_mask, level_index):
    land_float = land_mask.astype(jnp.float32)
    one_hot = (level_index[:, None] == jnp.arange(NCOEF, dtype=jnp.int32)[None, :]).astype(jnp.float32)

    def closed(xin, wgt, bvec, lvec, gtab):
        return forward(xin, wgt, bvec, lvec, gtab, land_float, one_hot)
    result, pullback = jax.vjp(closed, field, weight, bias, land_bias, level_gain)
    grads = pullback(grad_out)
    return (grads[0], grads[1], grads[2], grads[3], grads[4])
```

```python
import jax
import jax.numpy as jnp
from jax import lax
from jax.sharding import Mesh
from jax.sharding import PartitionSpec as P

highest = lax.Precision.HIGHEST
SPACE = ("chip", "core")


def with_halo(array):
    count = lax.axis_size(SPACE)
    up = [(i, i + 1) for i in range(count - 1)]
    down = [(j, i) for i, j in up]
    before = lax.ppermute(array[-1:], SPACE, up)
    after = lax.ppermute(array[:1], SPACE, down)
    return jnp.concatenate([before, array, after], axis=0)


def wrap_lon(grid):
    return jnp.concatenate([grid[:, -1:], grid, grid[:, :1]], axis=1)


def to_local_order(x, q, n_chip):
    lead = x.shape[:-1]
    blk = x.shape[-1] // (2 * n_chip)
    xt = jnp.swapaxes(x.reshape(lead + (n_chip, 2, blk)), -3, -2)
    xt = jnp.where(q == 0, xt, xt[..., ::-1, :, :])
    return xt.reshape(x.shape)


def from_local_order(x, q, n_chip):
    lead = x.shape[:-1]
    blk = x.shape[-1] // (2 * n_chip)
    xt = x.reshape(lead + (2, n_chip, blk))
    xt = jnp.where(q == 0, xt, xt[..., ::-1, :, :])
    return jnp.swapaxes(xt, -3, -2).reshape(x.shape)


def conv3(grid, kernel, rhs_spec):
    return lax.conv_general_dilated(
        grid[None],
        kernel,
        (1, 1, 1),
        [(0, 0), (0, 0), (1, 1)],
        dimension_numbers=("NDHWC", rhs_spec, "NDHWC"),
        precision=highest,
    )[0]


def all_sum(x):
    count = lax.axis_size(SPACE)
    if count & (count - 1):
        return lax.psum(x, SPACE)
    bit = 1
    while bit < count:
        pairs = [(i, i ^ bit) for i in range(count)]
        x = x + lax.ppermute(x, SPACE, pairs)
        bit *= 2
    return x


def per_device(field, grad_out, weight, bias, land_bias, level_gain, land_mask, level_index):
    rows, lon_n, lev_n, chans = field.shape
    n_chip = lax.axis_size("chip")
    q = lax.axis_index("core")
    swap = [(0, 1), (1, 0)]
    land_float = land_mask.astype(jnp.float32)
    one_hot = (
        level_index[:, None] == jnp.arange(level_gain.shape[0], dtype=jnp.int32)[None, :]
    ).astype(jnp.float32)
    gains = jnp.dot(one_hot, level_gain, precision=highest)

    mine_w = lax.all_gather(weight, "chip", axis=0, tiled=True)
    other_w = lax.ppermute(mine_w, "core", swap)
    kernel = jnp.concatenate([mine_w, other_w], axis=0).reshape(chans, 3, 3, 3, chans)

    grid = to_local_order(wrap_lon(with_halo(field)), q, n_chip)

    def forward_conv(k):
        return conv3(grid, k, "IDHWO")

    conv, weight_pullback = jax.vjp(forward_conv, kernel)
    pre = conv + bias + land_float[:, :, None, None] * land_bias
    sigma = jax.nn.sigmoid(pre)
    active = pre * sigma
    delta = grad_out * gains * sigma * (1.0 + pre * (1.0 - sigma))

    local_bias = jnp.sum(delta, axis=(0, 1, 2))
    local_land = jnp.sum(land_float[:, :, None, None] * delta, axis=(0, 1, 2))
    per_level = jnp.sum(grad_out * active, axis=(0, 1))
    local_gain = jnp.dot(one_hot.T, per_level, precision=highest)
    sums = all_sum(jnp.concatenate([local_bias[None], local_land[None], local_gain], axis=0))

    delta_grid = wrap_lon(with_halo(delta))
    back = conv3(delta_grid, lax.rev(kernel, (1, 2, 3)), "ODHWI")
    grad_field = grad_out + from_local_order(back, q, n_chip)

    (dk,) = weight_pullback(delta)
    dk = dk.reshape(chans, 27, chans)
    half = chans // 2
    chip_sum = dk[:half] + lax.ppermute(dk[half:], "core", swap)
    grad_weight = lax.psum_scatter(chip_sum, "chip", scatter_dimension=0, tiled=True)
    return (grad_field, grad_weight, sums[0], sums[1], sums[2:])


def solution(mesh):
    groups, space = mesh.devices.shape
    split = Mesh(mesh.devices.reshape(groups, space // 2, 2), ("groups",) + SPACE)
    cells = P(("groups",) + SPACE, None, None, None)
    in_specs = (
        cells,
        cells,
        P(SPACE, None, None),
        P(),
        P(),
        P(),
        P(SPACE, None),
        P(),
    )
    out_specs = (
        cells,
        P(("groups",) + SPACE, None, None),
        P("groups"),
        P("groups"),
        P("groups", None),
    )
    return jax.shard_map(
        per_device, mesh=split, in_specs=in_specs, out_specs=out_specs, check_vma=False
    )
```

```python
import jax
import jax.numpy as jnp
from jax import lax
from jax.sharding import PartitionSpec as P

highest = lax.Precision.HIGHEST
high = lax.Precision.HIGH


def with_halo(array, sides, width):
    for axis, dim in sides:
        count, length = (lax.axis_size(axis), array.shape[dim])
        up = [(i, (i + 1) % count) for i in range(count - 1)]
        down = [(j, i) for i, j in up]
        last = lax.slice_in_dim(array, length - width, length, axis=dim)
        leading = lax.slice_in_dim(array, 0, width, axis=dim)
        before = lax.ppermute(last, axis, up)
        after = lax.ppermute(leading, axis, down)
        array = jnp.concatenate([before, array, after], axis=dim)
    return array


def wrap_levels(field):
    wrapped = jnp.concatenate([field[:, -1:], field, field[:, :1]], axis=1)
    return jnp.pad(wrapped, ((0, 0), (0, 0), (1, 1), (0, 0)))


def window_table(grid, out_rows, flipped):
    lon_n = grid.shape[1] - 2
    lev_n = grid.shape[2] - 2
    chans = grid.shape[3]
    windows = []
    for offset in range(27):
        lat_off, remainder = divmod(offset, 9)
        lon_off, lev_off = divmod(remainder, 3)
        if flipped:
            lat_off, lon_off, lev_off = (2 - lat_off, 2 - lon_off, 2 - lev_off)
        window = grid[
            lat_off : lat_off + out_rows, lon_off : lon_off + lon_n, lev_off : lev_off + lev_n
        ]
        windows.append(window.reshape(-1, chans))
    return jnp.stack(windows, axis=1)


def conv_piece(table, piece):
    return jnp.einsum("rop,poc->rc", table, piece, precision=high)


def back_piece(table, piece):
    return jnp.einsum("roc,qoc->rq", table, piece, precision=high)


def per_device(field, grad_out, weight, bias, land_bias, level_gain, land_mask, level_index):
    rows, lon_n, lev_n, chans = field.shape
    land_float = land_mask.astype(jnp.float32)
    one_hot = (
        level_index[:, None] == jnp.arange(level_gain.shape[0], dtype=jnp.int32)[None, :]
    ).astype(jnp.float32)
    gains = jnp.dot(one_hot, level_gain, precision=highest)
    full_weight = lax.all_gather(weight, "space", axis=0, tiled=True)
    grid_pre = wrap_levels(with_halo(field, (("space", 0),), 1))
    table_pre = window_table(grid_pre, rows, False)
    conv = conv_piece(table_pre, full_weight)
    conv = conv.reshape(rows, lon_n, lev_n, chans)
    pre = conv + bias + land_float[:, :, None, None] * land_bias
    sigma = jax.nn.sigmoid(pre)
    active = pre * sigma
    delta = grad_out * gains * sigma * (1.0 + pre * (1.0 - sigma))
    delta_pad = with_halo(delta, (("space", 0),), 1)
    delta_table = window_table(wrap_levels(delta_pad), rows, True)
    back = back_piece(delta_table, full_weight)
    grad_field = grad_out + back.reshape(rows, lon_n, lev_n, chans)
    local_bias = jnp.sum(delta, axis=(0, 1, 2))
    local_land = jnp.sum(land_float[:, :, None, None] * delta, axis=(0, 1, 2))
    per_level = jnp.sum(grad_out * active, axis=(0, 1))
    local_gain = jnp.dot(one_hot.T, per_level, precision=highest)
    sums = lax.psum(jnp.concatenate([local_bias[None], local_land[None], local_gain], axis=0), "space")
    sums, delta_flat = lax.optimization_barrier((sums, delta.reshape(-1, chans)))
    grad_weight = lax.psum_scatter(
        jnp.einsum("rop,rq->poq", table_pre, delta_flat, precision=high),
        "space",
        scatter_dimension=0,
        tiled=True,
    )
    return (grad_field, grad_weight, sums[0], sums[1], sums[2:])


def solution(mesh):
    in_specs = (
        P(("groups", "space"), None, None, None),
        P(("groups", "space"), None, None, None),
        P("space", None, None),
        P(),
        P(),
        P(),
        P("space", None),
        P(),
    )
    out_specs = (
        P(("groups", "space"), None, None, None),
        P(("groups", "space"), None, None),
        P("groups"),
        P("groups"),
        P("groups", None),
    )
    return jax.shard_map(
        per_device, mesh=mesh, in_specs=in_specs, out_specs=out_specs, check_vma=False
    )
```

```python
import jax
import jax.numpy as jnp
from jax import lax
from jax.sharding import PartitionSpec as P

highest = lax.Precision.HIGHEST
high = lax.Precision.HIGH


def with_halo(array, sides, width):
    for axis, dim in sides:
        count, length = (lax.axis_size(axis), array.shape[dim])
        up = [(i, (i + 1) % count) for i in range(count - 1)]
        down = [(j, i) for i, j in up]
        last = lax.slice_in_dim(array, length - width, length, axis=dim)
        leading = lax.slice_in_dim(array, 0, width, axis=dim)
        before = lax.ppermute(last, axis, up)
        after = lax.ppermute(leading, axis, down)
        array = jnp.concatenate([before, array, after], axis=dim)
    return array


def wrap_levels(field):
    wrapped = jnp.concatenate([field[:, -1:], field, field[:, :1]], axis=1)
    return jnp.pad(wrapped, ((0, 0), (0, 0), (1, 1), (0, 0)))


def window_table(grid, out_rows, flipped):
    lon_n = grid.shape[1] - 2
    lev_n = grid.shape[2] - 2
    chans = grid.shape[3]
    windows = []
    for offset in range(27):
        lat_off, remainder = divmod(offset, 9)
        lon_off, lev_off = divmod(remainder, 3)
        if flipped:
            lat_off, lon_off, lev_off = (2 - lat_off, 2 - lon_off, 2 - lev_off)
        window = grid[
            lat_off : lat_off + out_rows, lon_off : lon_off + lon_n, lev_off : lev_off + lev_n
        ]
        windows.append(window.reshape(-1, chans))
    return jnp.stack(windows, axis=1)


def conv_piece(table, piece):
    return jnp.einsum("rop,poc->rc", table, piece, precision=high)


def back_piece(table, piece):
    return jnp.einsum("roc,qoc->rq", table, piece, precision=high)


def per_device(field, grad_out, weight, bias, land_bias, level_gain, land_mask, level_index):
    rows, lon_n, lev_n, chans = field.shape
    land_float = land_mask.astype(jnp.float32)
    one_hot = (
        level_index[:, None] == jnp.arange(level_gain.shape[0], dtype=jnp.int32)[None, :]
    ).astype(jnp.float32)
    gains = jnp.dot(one_hot, level_gain, precision=highest)
    full_weight = lax.all_gather(weight, "space", axis=0, tiled=True)
    grid_pre = wrap_levels(with_halo(field, (("space", 0),), 1))
    table_pre = window_table(grid_pre, rows, False)
    conv = conv_piece(table_pre, full_weight)
    conv = conv.reshape(rows, lon_n, lev_n, chans)
    pre = conv + bias + land_float[:, :, None, None] * land_bias
    sigma = jax.nn.sigmoid(pre)
    active = pre * sigma
    delta = grad_out * gains * sigma * (1.0 + pre * (1.0 - sigma))
    delta_pad = with_halo(delta, (("space", 0),), 1)
    delta_table = window_table(wrap_levels(delta_pad), rows, True)
    back = back_piece(delta_table, full_weight)
    grad_field = grad_out + back.reshape(rows, lon_n, lev_n, chans)
    local_bias = jnp.sum(delta, axis=(0, 1, 2))
    local_land = jnp.sum(land_float[:, :, None, None] * delta, axis=(0, 1, 2))
    per_level = jnp.sum(grad_out * active, axis=(0, 1))
    local_gain = jnp.dot(one_hot.T, per_level, precision=highest)
    partial = jnp.concatenate([local_bias[None], local_land[None], local_gain], axis=0)
    partial = jnp.pad(partial, ((0, 64 - partial.shape[0]), (0, 0)))
    sums = jnp.sum(lax.all_gather(partial, "space", axis=0, tiled=False), axis=0)
    delta_flat = delta.reshape(-1, chans)
    grad_weight = lax.psum_scatter(
        jnp.einsum("rq,rop->poq", delta_flat, table_pre, precision=high),
        "space",
        scatter_dimension=0,
        tiled=True,
    )
    return (grad_field, grad_weight, sums[0], sums[1], sums[2 : 2 + local_gain.shape[0]])


def solution(mesh):
    in_specs = (
        P(("groups", "space"), None, None, None),
        P(("groups", "space"), None, None, None),
        P("space", None, None),
        P(),
        P(),
        P(),
        P("space", None),
        P(),
    )
    out_specs = (
        P(("groups", "space"), None, None, None),
        P(("groups", "space"), None, None),
        P("groups"),
        P("groups"),
        P("groups", None),
    )
    return jax.shard_map(
        per_device, mesh=mesh, in_specs=in_specs, out_specs=out_specs, check_vma=False
    )
```

```python
import jax
import jax.numpy as jnp
from jax import lax
from jax.sharding import PartitionSpec as P

highest = lax.Precision.HIGHEST
high = lax.Precision.HIGH


def with_halo(array, sides, width):
    for axis, dim in sides:
        count, length = (lax.axis_size(axis), array.shape[dim])
        up = [(i, (i + 1) % count) for i in range(count - 1)]
        down = [(j, i) for i, j in up]
        last = lax.slice_in_dim(array, length - width, length, axis=dim)
        leading = lax.slice_in_dim(array, 0, width, axis=dim)
        before = lax.ppermute(last, axis, up)
        after = lax.ppermute(leading, axis, down)
        array = jnp.concatenate([before, array, after], axis=dim)
    return array


def wrap_levels(field):
    wrapped = jnp.concatenate([field[:, -1:], field, field[:, :1]], axis=1)
    return jnp.pad(wrapped, ((0, 0), (0, 0), (1, 1), (0, 0)))


def window_table(grid, out_rows, flipped):
    lon_n = grid.shape[1] - 2
    lev_n = grid.shape[2] - 2
    chans = grid.shape[3]
    windows = []
    for offset in range(27):
        lat_off, remainder = divmod(offset, 9)
        lon_off, lev_off = divmod(remainder, 3)
        if flipped:
            lat_off, lon_off, lev_off = (2 - lat_off, 2 - lon_off, 2 - lev_off)
        window = grid[
            lat_off : lat_off + out_rows, lon_off : lon_off + lon_n, lev_off : lev_off + lev_n
        ]
        windows.append(window.reshape(-1, chans))
    return jnp.stack(windows, axis=1)


def conv_piece(table, piece):
    return jnp.einsum("rop,poc->rc", table, piece, precision=high)


def back_piece(table, piece):
    return jnp.einsum("roc,qoc->rq", table, piece, precision=high)


def all_sum(x):
    count = lax.axis_size("space")
    if count & (count - 1):
        return lax.psum(x, "space")
    bit = 1
    while bit < count:
        x = x + lax.ppermute(x, "space", [(i, i ^ bit) for i in range(count)])
        bit *= 2
    return x


def per_device(field, grad_out, weight, bias, land_bias, level_gain, land_mask, level_index):
    rows, lon_n, lev_n, chans = field.shape
    land_float = land_mask.astype(jnp.float32)
    one_hot = (
        level_index[:, None] == jnp.arange(level_gain.shape[0], dtype=jnp.int32)[None, :]
    ).astype(jnp.float32)
    gains = jnp.dot(one_hot, level_gain, precision=highest)
    full_weight = lax.all_gather(weight, "space", axis=0, tiled=True)
    grid_pre = wrap_levels(with_halo(field, (("space", 0),), 1))
    table_pre = window_table(grid_pre, rows, False)
    conv = conv_piece(table_pre, full_weight)
    conv = conv.reshape(rows, lon_n, lev_n, chans)
    pre = conv + bias + land_float[:, :, None, None] * land_bias
    sigma = jax.nn.sigmoid(pre)
    active = pre * sigma
    delta = grad_out * gains * sigma * (1.0 + pre * (1.0 - sigma))
    delta_pad = with_halo(delta, (("space", 0),), 1)
    delta_table = window_table(wrap_levels(delta_pad), rows, True)
    back = back_piece(delta_table, full_weight)
    grad_field = grad_out + back.reshape(rows, lon_n, lev_n, chans)
    local_bias = jnp.sum(delta, axis=(0, 1, 2))
    local_land = jnp.sum(land_float[:, :, None, None] * delta, axis=(0, 1, 2))
    per_level = jnp.sum(grad_out * active, axis=(0, 1))
    local_gain = jnp.dot(one_hot.T, per_level, precision=highest)
    sums = all_sum(jnp.concatenate([local_bias[None], local_land[None], local_gain], axis=0))
    delta_flat = delta.reshape(-1, chans)
    grad_weight = lax.psum_scatter(
        jnp.einsum("rq,rop->poq", delta_flat, table_pre, precision=high),
        "space",
        scatter_dimension=0,
        tiled=True,
    )
    return (grad_field, grad_weight, sums[0], sums[1], sums[2 : 2 + local_gain.shape[0]])


def solution(mesh):
    in_specs = (
        P(("groups", "space"), None, None, None),
        P(("groups", "space"), None, None, None),
        P("space", None, None),
        P(),
        P(),
        P(),
        P("space", None),
        P(),
    )
    out_specs = (
        P(("groups", "space"), None, None, None),
        P(("groups", "space"), None, None),
        P("groups"),
        P("groups"),
        P("groups", None),
    )
    return jax.shard_map(
        per_device, mesh=mesh, in_specs=in_specs, out_specs=out_specs, check_vma=False
    )
```

```python
import jax
import jax.numpy as jnp
from jax import lax
from jax.sharding import PartitionSpec as P

highest = lax.Precision.HIGHEST
high = lax.Precision.HIGH


def with_halo(array, sides, width):
    for axis, dim in sides:
        count, length = (lax.axis_size(axis), array.shape[dim])
        up = [(i, (i + 1) % count) for i in range(count - 1)]
        down = [(j, i) for i, j in up]
        last = lax.slice_in_dim(array, length - width, length, axis=dim)
        leading = lax.slice_in_dim(array, 0, width, axis=dim)
        before = lax.ppermute(last, axis, up)
        after = lax.ppermute(leading, axis, down)
        array = jnp.concatenate([before, array, after], axis=dim)
    return array


def wrap_levels(field):
    wrapped = jnp.concatenate([field[:, -1:], field, field[:, :1]], axis=1)
    return jnp.pad(wrapped, ((0, 0), (0, 0), (1, 1), (0, 0)))


def window_table(grid, out_rows, flipped):
    lon_n = grid.shape[1] - 2
    lev_n = grid.shape[2] - 2
    chans = grid.shape[3]
    windows = []
    for offset in range(27):
        lat_off, remainder = divmod(offset, 9)
        lon_off, lev_off = divmod(remainder, 3)
        if flipped:
            lat_off, lon_off, lev_off = (2 - lat_off, 2 - lon_off, 2 - lev_off)
        window = grid[
            lat_off : lat_off + out_rows, lon_off : lon_off + lon_n, lev_off : lev_off + lev_n
        ]
        windows.append(window.reshape(-1, chans))
    return jnp.stack(windows, axis=1)


def conv_piece(table, piece):
    return jnp.einsum("rop,poc->rc", table, piece, precision=high)


def back_piece(table, piece):
    return jnp.einsum("roc,qoc->rq", table, piece, precision=high)


def all_sum(x):
    count = lax.axis_size("space")
    if count & (count - 1):
        return lax.psum(x, "space")
    bit = 1
    while bit < count:
        x = x + lax.ppermute(x, "space", [(i, i ^ bit) for i in range(count)])
        bit *= 2
    return x


def per_device(field, grad_out, weight, bias, land_bias, level_gain, land_mask, level_index):
    rows, lon_n, lev_n, chans = field.shape
    land_float = land_mask.astype(jnp.float32)
    one_hot = (
        level_index[:, None] == jnp.arange(level_gain.shape[0], dtype=jnp.int32)[None, :]
    ).astype(jnp.float32)
    gains = jnp.dot(one_hot, level_gain, precision=highest)
    full_weight = lax.all_gather(weight, "space", axis=0, tiled=True)
    grid_pre = wrap_levels(with_halo(field, (("space", 0),), 1))
    table_pre = window_table(grid_pre, rows, False)
    conv = conv_piece(table_pre, full_weight)
    conv = conv.reshape(rows, lon_n, lev_n, chans)
    pre = conv + bias + land_float[:, :, None, None] * land_bias
    sigma = jax.nn.sigmoid(pre)
    active = pre * sigma
    delta = grad_out * gains * sigma * (1.0 + pre * (1.0 - sigma))
    delta_pad = with_halo(delta, (("space", 0),), 1)
    delta_table = window_table(wrap_levels(delta_pad), rows, True)
    back = back_piece(delta_table, full_weight)
    grad_field = grad_out + back.reshape(rows, lon_n, lev_n, chans)
    local_bias = jnp.sum(delta, axis=(0, 1, 2))
    local_land = jnp.sum(land_float[:, :, None, None] * delta, axis=(0, 1, 2))
    per_level = jnp.sum(grad_out * active, axis=(0, 1))
    local_gain = jnp.dot(one_hot.T, per_level, precision=highest)
    sums = all_sum(jnp.concatenate([local_bias[None], local_land[None], local_gain], axis=0))
    delta_flat = delta.reshape(-1, chans)
    count = lax.axis_size("space")
    terms = jnp.einsum("rq,rop->poq", delta_flat, table_pre, precision=high)
    terms = terms.reshape((count, chans // count) + terms.shape[1:])
    grad_weight = jnp.sum(lax.all_to_all(terms, "space", 0, 0, tiled=False), axis=0)
    return (grad_field, grad_weight, sums[0], sums[1], sums[2 : 2 + local_gain.shape[0]])


def solution(mesh):
    in_specs = (
        P(("groups", "space"), None, None, None),
        P(("groups", "space"), None, None, None),
        P("space", None, None),
        P(),
        P(),
        P(),
        P("space", None),
        P(),
    )
    out_specs = (
        P(("groups", "space"), None, None, None),
        P(("groups", "space"), None, None),
        P("groups"),
        P("groups"),
        P("groups", None),
    )
    return jax.shard_map(
        per_device, mesh=mesh, in_specs=in_specs, out_specs=out_specs, check_vma=False
    )
```

```python
import jax
import jax.numpy as jnp
from jax import lax
from jax.sharding import PartitionSpec as P

highest = lax.Precision.HIGHEST
high = lax.Precision.HIGH


def with_halo(array, sides, width):
    for axis, dim in sides:
        count, length = (lax.axis_size(axis), array.shape[dim])
        up = [(i, (i + 1) % count) for i in range(count - 1)]
        down = [(j, i) for i, j in up]
        last = lax.slice_in_dim(array, length - width, length, axis=dim)
        leading = lax.slice_in_dim(array, 0, width, axis=dim)
        before = lax.ppermute(last, axis, up)
        after = lax.ppermute(leading, axis, down)
        array = jnp.concatenate([before, array, after], axis=dim)
    return array


def wrap_levels(field):
    wrapped = jnp.concatenate([field[:, -1:], field, field[:, :1]], axis=1)
    return jnp.pad(wrapped, ((0, 0), (0, 0), (1, 1), (0, 0)))


def window_table(grid, out_rows, flipped):
    lon_n = grid.shape[1] - 2
    lev_n = grid.shape[2] - 2
    chans = grid.shape[3]
    windows = []
    for offset in range(27):
        lat_off, remainder = divmod(offset, 9)
        lon_off, lev_off = divmod(remainder, 3)
        if flipped:
            lat_off, lon_off, lev_off = (2 - lat_off, 2 - lon_off, 2 - lev_off)
        window = grid[
            lat_off : lat_off + out_rows, lon_off : lon_off + lon_n, lev_off : lev_off + lev_n
        ]
        windows.append(window.reshape(-1, chans))
    return jnp.stack(windows, axis=1)


def conv_piece(table, piece):
    return jnp.einsum("rop,poc->rc", table, piece, precision=high)


def back_piece(table, piece):
    return jnp.einsum("roc,qoc->rq", table, piece, precision=high)


def all_sum(x):
    count = lax.axis_size("space")
    if count & (count - 1):
        return lax.psum(x, "space")
    bit = 1
    while bit < count:
        x = x + lax.ppermute(x, "space", [(i, i ^ bit) for i in range(count)])
        bit *= 2
    return x


def per_device(field, grad_out, weight, bias, land_bias, level_gain, land_mask, level_index):
    rows, lon_n, lev_n, chans = field.shape
    land_float = land_mask.astype(jnp.float32)
    one_hot = (
        level_index[:, None] == jnp.arange(level_gain.shape[0], dtype=jnp.int32)[None, :]
    ).astype(jnp.float32)
    gains = jnp.dot(one_hot, level_gain, precision=highest)
    full_weight = lax.all_gather(weight, "space", axis=0, tiled=True)
    grid_pre = wrap_levels(with_halo(field, (("space", 0),), 1))
    table_pre = window_table(grid_pre, rows, False)
    conv = conv_piece(table_pre, full_weight)
    conv = conv.reshape(rows, lon_n, lev_n, chans)
    pre = conv + bias + land_float[:, :, None, None] * land_bias
    sigma = jax.nn.sigmoid(pre)
    active = pre * sigma
    delta = grad_out * gains * sigma * (1.0 + pre * (1.0 - sigma))
    delta_pad = with_halo(delta, (("space", 0),), 1)
    delta_table = window_table(wrap_levels(delta_pad), rows, True)
    back = back_piece(delta_table, full_weight)
    grad_field = grad_out + back.reshape(rows, lon_n, lev_n, chans)
    local_bias = jnp.sum(delta, axis=(0, 1, 2))
    local_land = jnp.sum(land_float[:, :, None, None] * delta, axis=(0, 1, 2))
    per_level = jnp.sum(grad_out * active, axis=(0, 1))
    local_gain = jnp.dot(one_hot.T, per_level, precision=highest)
    sums = all_sum(jnp.concatenate([local_bias[None], local_land[None], local_gain], axis=0))
    delta_flat = delta.reshape(-1, chans)
    grad_weight = lax.psum_scatter(
        jnp.einsum("rq,rop->opq", delta_flat, table_pre, precision=high),
        "space",
        scatter_dimension=1,
        tiled=True,
    )
    grad_weight = jnp.transpose(grad_weight, (1, 0, 2))
    return (grad_field, grad_weight, sums[0], sums[1], sums[2 : 2 + local_gain.shape[0]])


def solution(mesh):
    in_specs = (
        P(("groups", "space"), None, None, None),
        P(("groups", "space"), None, None, None),
        P("space", None, None),
        P(),
        P(),
        P(),
        P("space", None),
        P(),
    )
    out_specs = (
        P(("groups", "space"), None, None, None),
        P(("groups", "space"), None, None),
        P("groups"),
        P("groups"),
        P("groups", None),
    )
    return jax.shard_map(
        per_device, mesh=mesh, in_specs=in_specs, out_specs=out_specs, check_vma=False
    )
```

```python
import jax
import jax.numpy as jnp
from jax import lax
from jax.sharding import PartitionSpec as P

highest = lax.Precision.HIGHEST
high = lax.Precision.HIGH


def with_halo(array, sides, width):
    for axis, dim in sides:
        count, length = (lax.axis_size(axis), array.shape[dim])
        up = [(i, (i + 1) % count) for i in range(count - 1)]
        down = [(j, i) for i, j in up]
        last = lax.slice_in_dim(array, length - width, length, axis=dim)
        leading = lax.slice_in_dim(array, 0, width, axis=dim)
        before = lax.ppermute(last, axis, up)
        after = lax.ppermute(leading, axis, down)
        array = jnp.concatenate([before, array, after], axis=dim)
    return array


def wrap_levels(field):
    wrapped = jnp.concatenate([field[:, -1:], field, field[:, :1]], axis=1)
    return jnp.pad(wrapped, ((0, 0), (0, 0), (1, 1), (0, 0)))


def window_table(grid, out_rows, flipped):
    lon_n = grid.shape[1] - 2
    lev_n = grid.shape[2] - 2
    chans = grid.shape[3]
    windows = []
    for offset in range(27):
        lat_off, remainder = divmod(offset, 9)
        lon_off, lev_off = divmod(remainder, 3)
        if flipped:
            lat_off, lon_off, lev_off = (2 - lat_off, 2 - lon_off, 2 - lev_off)
        window = grid[
            lat_off : lat_off + out_rows, lon_off : lon_off + lon_n, lev_off : lev_off + lev_n
        ]
        windows.append(window.reshape(-1, chans))
    return jnp.stack(windows, axis=1)


def conv_piece(table, piece):
    return jnp.einsum("rop,poc->rc", table, piece, precision=high)


def back_piece(table, piece):
    return jnp.einsum("roc,qoc->rq", table, piece, precision=high)


def all_sum(x):
    count = lax.axis_size("space")
    if count & (count - 1):
        return lax.psum(x, "space")
    bit = 1
    while bit < count:
        x = x + lax.ppermute(x, "space", [(i, i ^ bit) for i in range(count)])
        bit *= 2
    return x


def split_bf16(x):
    hi = lax.reduce_precision(x, exponent_bits=8, mantissa_bits=7)
    return hi.astype(jnp.bfloat16), (x - hi).astype(jnp.bfloat16)


def dot3(spec, a_parts, b_parts):
    (a_hi, a_lo), (b_hi, b_lo) = a_parts, b_parts
    part = lambda x, y: jnp.einsum(spec, x, y, preferred_element_type=jnp.float32)
    return part(a_hi, b_hi) + (part(a_hi, b_lo) + part(a_lo, b_hi))


def per_device(field, grad_out, weight, bias, land_bias, level_gain, land_mask, level_index):
    rows, lon_n, lev_n, chans = field.shape
    land_float = land_mask.astype(jnp.float32)
    one_hot = (
        level_index[:, None] == jnp.arange(level_gain.shape[0], dtype=jnp.int32)[None, :]
    ).astype(jnp.float32)
    gains = jnp.dot(one_hot, level_gain, precision=highest)
    full_weight = lax.all_gather(weight, "space", axis=0, tiled=True)
    grid_pre = wrap_levels(with_halo(field, (("space", 0),), 1))
    grid_hi, grid_lo = split_bf16(grid_pre)
    table_pre = (window_table(grid_hi, rows, False), window_table(grid_lo, rows, False))
    conv = dot3("rop,poc->rc", table_pre, split_bf16(full_weight))
    conv = conv.reshape(rows, lon_n, lev_n, chans)
    pre = conv + bias + land_float[:, :, None, None] * land_bias
    sigma = jax.nn.sigmoid(pre)
    active = pre * sigma
    delta = grad_out * gains * sigma * (1.0 + pre * (1.0 - sigma))
    delta_pad = with_halo(delta, (("space", 0),), 1)
    delta_table = window_table(wrap_levels(delta_pad), rows, True)
    back = back_piece(delta_table, full_weight)
    grad_field = grad_out + back.reshape(rows, lon_n, lev_n, chans)
    local_bias = jnp.sum(delta, axis=(0, 1, 2))
    local_land = jnp.sum(land_float[:, :, None, None] * delta, axis=(0, 1, 2))
    per_level = jnp.sum(grad_out * active, axis=(0, 1))
    local_gain = jnp.dot(one_hot.T, per_level, precision=highest)
    sums = all_sum(jnp.concatenate([local_bias[None], local_land[None], local_gain], axis=0))
    delta_flat = delta.reshape(-1, chans)
    grad_weight = lax.psum_scatter(
        dot3("rq,rop->opq", split_bf16(delta_flat), table_pre),
        "space",
        scatter_dimension=1,
        tiled=True,
    )
    grad_weight = jnp.transpose(grad_weight, (1, 0, 2))
    return (grad_field, grad_weight, sums[0], sums[1], sums[2 : 2 + local_gain.shape[0]])


def solution(mesh):
    in_specs = (
        P(("groups", "space"), None, None, None),
        P(("groups", "space"), None, None, None),
        P("space", None, None),
        P(),
        P(),
        P(),
        P("space", None),
        P(),
    )
    out_specs = (
        P(("groups", "space"), None, None, None),
        P(("groups", "space"), None, None),
        P("groups"),
        P("groups"),
        P("groups", None),
    )
    return jax.shard_map(
        per_device, mesh=mesh, in_specs=in_specs, out_specs=out_specs, check_vma=False
    )
```

```python
import jax
import jax.numpy as jnp
from jax import lax
from jax.sharding import PartitionSpec as P

highest = lax.Precision.HIGHEST
high = lax.Precision.HIGH


def with_halo(array, sides, width):
    for axis, dim in sides:
        count, length = (lax.axis_size(axis), array.shape[dim])
        up = [(i, (i + 1) % count) for i in range(count - 1)]
        down = [(j, i) for i, j in up]
        last = lax.slice_in_dim(array, length - width, length, axis=dim)
        leading = lax.slice_in_dim(array, 0, width, axis=dim)
        before = lax.ppermute(last, axis, up)
        after = lax.ppermute(leading, axis, down)
        array = jnp.concatenate([before, array, after], axis=dim)
    return array


def wrap_levels(field):
    wrapped = jnp.concatenate([field[:, -1:], field, field[:, :1]], axis=1)
    return jnp.pad(wrapped, ((0, 0), (0, 0), (1, 1), (0, 0)))


def window_table(grid, out_rows, flipped):
    lon_n = grid.shape[1] - 2
    lev_n = grid.shape[2] - 2
    chans = grid.shape[3]
    windows = []
    for offset in range(27):
        lat_off, remainder = divmod(offset, 9)
        lon_off, lev_off = divmod(remainder, 3)
        if flipped:
            lat_off, lon_off, lev_off = (2 - lat_off, 2 - lon_off, 2 - lev_off)
        window = grid[
            lat_off : lat_off + out_rows, lon_off : lon_off + lon_n, lev_off : lev_off + lev_n
        ]
        windows.append(window.reshape(-1, chans))
    return jnp.stack(windows, axis=1)


def conv_piece(table, piece):
    return jnp.einsum("rop,poc->rc", table, piece, precision=high)


def back_piece(table, piece):
    return jnp.einsum("roc,qoc->rq", table, piece, precision=high)


def stacked_product(delta_flat, table):
    d_hi, d_lo = split_bf16(delta_flat)
    t_hi, t_lo = split_bf16(table)
    lhs = jnp.concatenate([d_hi, d_hi, d_lo], axis=0)
    rhs = jnp.concatenate([t_hi, t_lo, t_hi], axis=0)
    return jnp.einsum("rq,rop->opq", lhs, rhs, preferred_element_type=jnp.float32)


def all_sum(x):
    count = lax.axis_size("space")
    if count & (count - 1):
        return lax.psum(x, "space")
    bit = 1
    while bit < count:
        x = x + lax.ppermute(x, "space", [(i, i ^ bit) for i in range(count)])
        bit *= 2
    return x


def split_bf16(x):
    hi = lax.reduce_precision(x, exponent_bits=8, mantissa_bits=7)
    return hi.astype(jnp.bfloat16), (x - hi).astype(jnp.bfloat16)


def per_device(field, grad_out, weight, bias, land_bias, level_gain, land_mask, level_index):
    rows, lon_n, lev_n, chans = field.shape
    land_float = land_mask.astype(jnp.float32)
    one_hot = (
        level_index[:, None] == jnp.arange(level_gain.shape[0], dtype=jnp.int32)[None, :]
    ).astype(jnp.float32)
    gains = jnp.dot(one_hot, level_gain, precision=highest)
    full_weight = lax.all_gather(weight, "space", axis=0, tiled=True)
    grid_pre = wrap_levels(with_halo(field, (("space", 0),), 1))
    table_pre = window_table(grid_pre, rows, False)
    conv = conv_piece(table_pre, full_weight)
    conv = conv.reshape(rows, lon_n, lev_n, chans)
    pre = conv + bias + land_float[:, :, None, None] * land_bias
    sigma = jax.nn.sigmoid(pre)
    active = pre * sigma
    delta = grad_out * gains * sigma * (1.0 + pre * (1.0 - sigma))
    delta_pad = with_halo(delta, (("space", 0),), 1)
    delta_table = window_table(wrap_levels(delta_pad), rows, True)
    back = back_piece(delta_table, full_weight)
    grad_field = grad_out + back.reshape(rows, lon_n, lev_n, chans)
    local_bias = jnp.sum(delta, axis=(0, 1, 2))
    local_land = jnp.sum(land_float[:, :, None, None] * delta, axis=(0, 1, 2))
    per_level = jnp.sum(grad_out * active, axis=(0, 1))
    local_gain = jnp.dot(one_hot.T, per_level, precision=highest)
    sums = all_sum(jnp.concatenate([local_bias[None], local_land[None], local_gain], axis=0))
    delta_flat = delta.reshape(-1, chans)
    grad_weight = lax.psum_scatter(
        stacked_product(delta_flat, table_pre),
        "space",
        scatter_dimension=1,
        tiled=True,
    )
    grad_weight = jnp.transpose(grad_weight, (1, 0, 2))
    return (grad_field, grad_weight, sums[0], sums[1], sums[2 : 2 + local_gain.shape[0]])


def solution(mesh):
    in_specs = (
        P(("groups", "space"), None, None, None),
        P(("groups", "space"), None, None, None),
        P("space", None, None),
        P(),
        P(),
        P(),
        P("space", None),
        P(),
    )
    out_specs = (
        P(("groups", "space"), None, None, None),
        P(("groups", "space"), None, None),
        P("groups"),
        P("groups"),
        P("groups", None),
    )
    return jax.shard_map(
        per_device, mesh=mesh, in_specs=in_specs, out_specs=out_specs, check_vma=False
    )
```

```python
import jax
import jax.numpy as jnp
from jax import lax
from jax.sharding import PartitionSpec as P

highest = lax.Precision.HIGHEST
high = lax.Precision.HIGH


def with_halo(array, sides, width):
    for axis, dim in sides:
        count, length = (lax.axis_size(axis), array.shape[dim])
        up = [(i, (i + 1) % count) for i in range(count - 1)]
        down = [(j, i) for i, j in up]
        last = lax.slice_in_dim(array, length - width, length, axis=dim)
        leading = lax.slice_in_dim(array, 0, width, axis=dim)
        before = lax.ppermute(last, axis, up)
        after = lax.ppermute(leading, axis, down)
        array = jnp.concatenate([before, array, after], axis=dim)
    return array


def wrap_levels(field):
    wrapped = jnp.concatenate([field[:, -1:], field, field[:, :1]], axis=1)
    return jnp.pad(wrapped, ((0, 0), (0, 0), (1, 1), (0, 0)))


def window_table(grid, out_rows, flipped):
    lon_n = grid.shape[1] - 2
    lev_n = grid.shape[2] - 2
    chans = grid.shape[3]
    windows = []
    for offset in range(27):
        lat_off, remainder = divmod(offset, 9)
        lon_off, lev_off = divmod(remainder, 3)
        if flipped:
            lat_off, lon_off, lev_off = (2 - lat_off, 2 - lon_off, 2 - lev_off)
        window = grid[
            lat_off : lat_off + out_rows, lon_off : lon_off + lon_n, lev_off : lev_off + lev_n
        ]
        windows.append(window.reshape(-1, chans))
    return jnp.stack(windows, axis=1)


def conv_piece(table, piece):
    return jnp.einsum("rop,poc->rc", table, piece, precision=high)


def back_piece(table, piece):
    return jnp.einsum("roc,qoc->rq", table, piece, precision=high)


def stacked_conv(table, weight):
    t_hi, t_lo = split_bf16(table)
    w_hi, w_lo = split_bf16(weight)
    lhs = jnp.concatenate([t_hi, t_hi, t_lo], axis=2)
    rhs = jnp.concatenate([w_hi, w_lo, w_hi], axis=0)
    return jnp.einsum("rop,poc->rc", lhs, rhs, preferred_element_type=jnp.float32)


def stacked_product(delta_flat, table):
    d_hi, d_lo = split_bf16(delta_flat)
    t_hi, t_lo = split_bf16(table)
    lhs = jnp.concatenate([d_hi, d_hi, d_lo], axis=0)
    rhs = jnp.concatenate([t_hi, t_lo, t_hi], axis=0)
    return jnp.einsum("rq,rop->opq", lhs, rhs, preferred_element_type=jnp.float32)


def all_sum(x):
    count = lax.axis_size("space")
    if count & (count - 1):
        return lax.psum(x, "space")
    bit = 1
    while bit < count:
        x = x + lax.ppermute(x, "space", [(i, i ^ bit) for i in range(count)])
        bit *= 2
    return x


def split_bf16(x):
    hi = lax.reduce_precision(x, exponent_bits=8, mantissa_bits=7)
    return hi.astype(jnp.bfloat16), (x - hi).astype(jnp.bfloat16)


def per_device(field, grad_out, weight, bias, land_bias, level_gain, land_mask, level_index):
    rows, lon_n, lev_n, chans = field.shape
    land_float = land_mask.astype(jnp.float32)
    one_hot = (
        level_index[:, None] == jnp.arange(level_gain.shape[0], dtype=jnp.int32)[None, :]
    ).astype(jnp.float32)
    gains = jnp.dot(one_hot, level_gain, precision=highest)
    full_weight = lax.all_gather(weight, "space", axis=0, tiled=True)
    grid_pre = wrap_levels(with_halo(field, (("space", 0),), 1))
    table_pre = window_table(grid_pre, rows, False)
    conv = stacked_conv(table_pre, full_weight)
    conv = conv.reshape(rows, lon_n, lev_n, chans)
    pre = conv + bias + land_float[:, :, None, None] * land_bias
    sigma = jax.nn.sigmoid(pre)
    active = pre * sigma
    delta = grad_out * gains * sigma * (1.0 + pre * (1.0 - sigma))
    delta_pad = with_halo(delta, (("space", 0),), 1)
    delta_table = window_table(wrap_levels(delta_pad), rows, True)
    back = back_piece(delta_table, full_weight)
    grad_field = grad_out + back.reshape(rows, lon_n, lev_n, chans)
    local_bias = jnp.sum(delta, axis=(0, 1, 2))
    local_land = jnp.sum(land_float[:, :, None, None] * delta, axis=(0, 1, 2))
    per_level = jnp.sum(grad_out * active, axis=(0, 1))
    local_gain = jnp.dot(one_hot.T, per_level, precision=highest)
    sums = all_sum(jnp.concatenate([local_bias[None], local_land[None], local_gain], axis=0))
    delta_flat = delta.reshape(-1, chans)
    grad_weight = lax.psum_scatter(
        stacked_product(delta_flat, table_pre),
        "space",
        scatter_dimension=1,
        tiled=True,
    )
    grad_weight = jnp.transpose(grad_weight, (1, 0, 2))
    return (grad_field, grad_weight, sums[0], sums[1], sums[2 : 2 + local_gain.shape[0]])


def solution(mesh):
    in_specs = (
        P(("groups", "space"), None, None, None),
        P(("groups", "space"), None, None, None),
        P("space", None, None),
        P(),
        P(),
        P(),
        P("space", None),
        P(),
    )
    out_specs = (
        P(("groups", "space"), None, None, None),
        P(("groups", "space"), None, None),
        P("groups"),
        P("groups"),
        P("groups", None),
    )
    return jax.shard_map(
        per_device, mesh=mesh, in_specs=in_specs, out_specs=out_specs, check_vma=False
    )
```

```python
import jax
import jax.numpy as jnp
from jax import lax
from jax.sharding import PartitionSpec as P

highest = lax.Precision.HIGHEST
high = lax.Precision.HIGH


def with_halo(array, sides, width):
    for axis, dim in sides:
        count, length = (lax.axis_size(axis), array.shape[dim])
        up = [(i, (i + 1) % count) for i in range(count - 1)]
        down = [(j, i) for i, j in up]
        last = lax.slice_in_dim(array, length - width, length, axis=dim)
        leading = lax.slice_in_dim(array, 0, width, axis=dim)
        before = lax.ppermute(last, axis, up)
        after = lax.ppermute(leading, axis, down)
        array = jnp.concatenate([before, array, after], axis=dim)
    return array


def wrap_levels(field):
    wrapped = jnp.concatenate([field[:, -1:], field, field[:, :1]], axis=1)
    return jnp.pad(wrapped, ((0, 0), (0, 0), (1, 1), (0, 0)))


def window_table(grid, out_rows, flipped):
    lon_n = grid.shape[1] - 2
    lev_n = grid.shape[2] - 2
    chans = grid.shape[3]
    windows = []
    for offset in range(27):
        lat_off, remainder = divmod(offset, 9)
        lon_off, lev_off = divmod(remainder, 3)
        if flipped:
            lat_off, lon_off, lev_off = (2 - lat_off, 2 - lon_off, 2 - lev_off)
        window = grid[
            lat_off : lat_off + out_rows, lon_off : lon_off + lon_n, lev_off : lev_off + lev_n
        ]
        windows.append(window.reshape(-1, chans))
    return jnp.stack(windows, axis=1)


def conv_piece(table, piece):
    return jnp.einsum("rop,poc->rc", table, piece, precision=high)


def back_piece(table, piece):
    return jnp.einsum("roc,qoc->rq", table, piece, precision=high)


def stacked_product(delta_flat, table):
    d_hi, d_lo = split_bf16(delta_flat)
    t_hi, t_lo = split_bf16(table)
    lhs = jnp.concatenate([d_hi, d_hi, d_lo], axis=0)
    rhs = jnp.concatenate([t_hi, t_lo, t_hi], axis=0)
    return jnp.einsum("rq,rop->opq", lhs, rhs, preferred_element_type=jnp.float32)


def stacked_back(table, weight):
    t_hi, t_lo = split_bf16(table)
    w_hi, w_lo = split_bf16(weight)
    lhs = jnp.concatenate([t_hi, t_hi, t_lo], axis=2)
    rhs = jnp.concatenate([w_hi, w_lo, w_hi], axis=2)
    return jnp.einsum("roc,qoc->rq", lhs, rhs, preferred_element_type=jnp.float32)


def all_sum(x):
    count = lax.axis_size("space")
    if count & (count - 1):
        return lax.psum(x, "space")
    bit = 1
    while bit < count:
        x = x + lax.ppermute(x, "space", [(i, i ^ bit) for i in range(count)])
        bit *= 2
    return x


def split_bf16(x):
    hi = lax.reduce_precision(x, exponent_bits=8, mantissa_bits=7)
    return hi.astype(jnp.bfloat16), (x - hi).astype(jnp.bfloat16)


def per_device(field, grad_out, weight, bias, land_bias, level_gain, land_mask, level_index):
    rows, lon_n, lev_n, chans = field.shape
    land_float = land_mask.astype(jnp.float32)
    one_hot = (
        level_index[:, None] == jnp.arange(level_gain.shape[0], dtype=jnp.int32)[None, :]
    ).astype(jnp.float32)
    gains = jnp.dot(one_hot, level_gain, precision=highest)
    full_weight = lax.all_gather(weight, "space", axis=0, tiled=True)
    grid_pre = wrap_levels(with_halo(field, (("space", 0),), 1))
    table_pre = window_table(grid_pre, rows, False)
    conv = conv_piece(table_pre, full_weight)
    conv = conv.reshape(rows, lon_n, lev_n, chans)
    pre = conv + bias + land_float[:, :, None, None] * land_bias
    sigma = jax.nn.sigmoid(pre)
    active = pre * sigma
    delta = grad_out * gains * sigma * (1.0 + pre * (1.0 - sigma))
    delta_pad = with_halo(delta, (("space", 0),), 1)
    delta_table = window_table(wrap_levels(delta_pad), rows, True)
    back = stacked_back(delta_table, full_weight)
    grad_field = grad_out + back.reshape(rows, lon_n, lev_n, chans)
    local_bias = jnp.sum(delta, axis=(0, 1, 2))
    local_land = jnp.sum(land_float[:, :, None, None] * delta, axis=(0, 1, 2))
    per_level = jnp.sum(grad_out * active, axis=(0, 1))
    local_gain = jnp.dot(one_hot.T, per_level, precision=highest)
    sums = all_sum(jnp.concatenate([local_bias[None], local_land[None], local_gain], axis=0))
    delta_flat = delta.reshape(-1, chans)
    grad_weight = lax.psum_scatter(
        stacked_product(delta_flat, table_pre),
        "space",
        scatter_dimension=1,
        tiled=True,
    )
    grad_weight = jnp.transpose(grad_weight, (1, 0, 2))
    return (grad_field, grad_weight, sums[0], sums[1], sums[2 : 2 + local_gain.shape[0]])


def solution(mesh):
    in_specs = (
        P(("groups", "space"), None, None, None),
        P(("groups", "space"), None, None, None),
        P("space", None, None),
        P(),
        P(),
        P(),
        P("space", None),
        P(),
    )
    out_specs = (
        P(("groups", "space"), None, None, None),
        P(("groups", "space"), None, None),
        P("groups"),
        P("groups"),
        P("groups", None),
    )
    return jax.shard_map(
        per_device, mesh=mesh, in_specs=in_specs, out_specs=out_specs, check_vma=False
    )
```
